256 devices in a mesh: dp: 8 (over y, x_lo), expert: 32 (over x_hi, z, core).
Axes of the slice: x: 4 (x_hi: 2, x_lo: 2; x = x_hi * 2 + x_lo), y: 4, z: 8, core: 2. Of those that a mesh axis runs over, the one named last changes fastest.
Arguments:
- tokens: bfloat16 [32768, 2048], P(('dp', 'expert')), may hold values from -24 to 24
- out_grad: bfloat16 [32768, 2048], P(('dp', 'expert')), may hold values from -6 to 6
- expert_ids: int32 [32768, 8], P(('dp', 'expert')), may hold values from 0 to 63, all different within a row; in each aligned block of 128 rows (0 to 127, 128 to 255, ...) at most 18 rows name the same one
- route_probs: float32 [32768, 8], P(('dp', 'expert')), may hold values from 0.05 to 0.5
- gate_weight: bfloat16 [64, 2048, 384], P('expert'), may hold values from -0.125 to 0.125
- up_weight: bfloat16 [64, 2048, 384], P('expert'), may hold values from -0.125 to 0.125
- down_weight: bfloat16 [64, 384, 2048], P('expert'), may hold values from -0.3125 to 0.3125
Outputs:
- in_grad: bfloat16 [32768, 2048], P(('dp', 'expert'))
- grad_gate: bfloat16 [64, 2048, 384], P('expert', 'dp')
- grad_up: bfloat16 [64, 2048, 384], P('expert', 'dp')
- grad_down: bfloat16 [64, 384, 2048], P('expert', None, 'dp')
The draws below stay inside these ranges and needn't reach their ends.
Inputs may be any that keep to these rules, and one draw needn't show every extreme that they name: `expert_ids`: within the 128 tokens of one device no expert is named more than 18 times, a bound that some block reaches; a token names 8 different experts.
All inputs are finite; a program needn't handle non-finite values.
Results may differ from the reference program's by a relative error of at most 0.014.
Values may be sent and summed in bfloat16 or wider, within the bound.
No kernel may reach another device: no remote copies, remote signals or barrier semaphores. Data moves between devices by JAX's collectives and lax.ppermute only.
A program may use at most 128 MiB of HBM per device.

```python
import math
import jax
import jax.numpy as jnp
import numpy as np
from jax import lax

D = 2048
HID = 384
TOP = 8
TOK_DEV = 128
EXPERTS = 64
CAP = 18
TOKENS = 32768
N_DP = 8
N_EXPERT = 32


def spiked(result, rng, source, target, blocks, factor):
    owner, partner = [(jnp.arange(result.shape[position]) // (result.shape[position] // blocks)).reshape([-1 if axis == position else 1 for axis in range(result.ndim)]) for position in (source, target)]
    chosen = jax.random.permutation(rng, blocks)[partner]
    strong = (owner == chosen) | (owner == (partner + blocks // 2) % blocks)
    return jnp.where(strong, factor * result, result)


def block_levels(stream_key, dims, split, smallest, top_value):
    def one(axis_at, blocks):
        heights = jax.random.uniform(jax.random.fold_in(jax.random.fold_in(stream_key, 6), axis_at), (blocks,), jnp.float32, smallest / len(split), top_value / len(split))
        return jnp.repeat(jnp.exp(heights), dims[axis_at] // blocks).reshape((-1,) + (1,) * (len(dims) - axis_at - 1))

    gain = one(*split[0])
    for cut in split[1:]:
        gain = gain * one(*cut)
    return gain


def routed_block(key, own, number, rows, number_of, top, reach, slope):
    ranking = jax.random.permutation(key, number_of)
    packed, usual = load_shares(number_of, rows * top, reach, slope, True), load_shares(number_of, rows * top, reach, slope, False)
    places = jnp.arange(number_of)

    def named(lengths, offset_by):
        used = int((lengths > 0).sum())
        fixed = max(1, used // 4)
        passed = fixed + (places - fixed + offset_by * (used - fixed)) % max(1, number_of - fixed)
        return jnp.zeros((number_of,), jnp.int32).at[ranking[jnp.where(places < fixed, places, passed)]].set(jnp.asarray(lengths, jnp.int32))

    lengths = jnp.where(number % 4 == 0, named(packed, number // 4), named(usual, number - number // 4 - 1))
    mixed = jax.random.permutation(jax.random.fold_in(own, 3), number_of)
    source_of, taker = mixed[0:number_of // 2 * 2:2], mixed[1:number_of // 2 * 2:2]
    room = jnp.minimum(lengths[source_of] - 1, reach - lengths[taker]) // 2
    room = jnp.where((source_of == ranking[0]) | (taker == ranking[0]) | (lengths[taker] == 0), 0, jnp.maximum(room, 0))
    passed = jax.random.randint(jax.random.fold_in(own, 4), (number_of // 2,), 0, 1 << 20) % (room + 1)
    lengths = lengths.at[source_of].add(-passed).at[taker].add(passed)
    members = jnp.searchsorted(jnp.cumsum(lengths), jnp.arange(rows * top), side="right").astype(jnp.int32)
    grid = members.reshape(top, rows).T
    grid = grid[jax.random.permutation(jax.random.fold_in(own, 1), rows)]
    offset_by = jax.random.randint(jax.random.fold_in(own, 2), (rows, 1), 0, top)
    return jnp.take_along_axis(grid, (jnp.arange(top)[None, :] + offset_by) % top, axis=1)


def load_shares(count, total, most, slope, full):
    weights = [(1 << 20) // math.isqrt(standing ** slope) + 1 for standing in range(1, count + 1)]
    largest = most if full else min(most, max(-(-total // count), total * weights[0] // sum(weights)))
    least = 1 if total - largest >= count - 1 else 0
    given, rest = [largest] + [least] * (count - 1), total - largest - least * (count - 1)
    while rest > 0:
        movable = [i for i in range(1, count) if given[i] < largest] or [i for i in range(1, count) if given[i] < most]
        whole, left = sum([weights[i] for i in movable]), rest
        for i in movable:
            addition = min(most - given[i], max(1, left * weights[i] // whole), rest)
            given[i] = given[i] + addition
            rest = rest - addition
    return np.array(given)


def scatter_about(stream_key, dims, width, limit, pieces=(), held_as=jnp.bfloat16):
    drawn = width * jax.random.normal(stream_key, dims, jnp.float32)
    if pieces:
        drawn = drawn * block_levels(stream_key, dims, pieces, -0.22, 0.18)
    return jnp.clip(drawn, -limit, limit).astype(held_as)


def noise_with(key, shape, width, most, shards, heavy, held_as=jnp.bfloat16):
    result = width * jax.random.normal(key, shape, jnp.float32)
    if shards:
        result = result * block_levels(key, shape, shards, -0.22, 0.18)
    return jnp.clip(spiked(result, jax.random.fold_in(key, 3), *heavy), -most, most).astype(held_as)


def setup_inputs(seed: int = 0) -> dict:
    seeds = jax.random.split(jax.random.key(seed), 8)
    tokens = noise_with(seeds[0], (TOKENS, D), 1.0, 24.0, ((0, 256),), (0, 1, 256, 6.0))
    out_grad = scatter_about(seeds[1], (TOKENS, D), 1.0, 6.0, ((0, 256),))
    expert_ids_keys = jax.random.split(jax.random.fold_in(seeds[2], 1), TOKENS // TOK_DEV)
    expert_ids_turns = jax.random.permutation(jax.random.fold_in(seeds[2], 3), TOKENS // TOK_DEV)
    expert_ids = jax.vmap(lambda own, number: routed_block(jax.random.fold_in(seeds[2], 2), own, number, TOK_DEV, EXPERTS, TOP, CAP, 2))(expert_ids_keys, expert_ids_turns).reshape((TOKENS, TOP))
    route_probs = jnp.clip(jnp.exp(math.log(0.5) - 2.3025851 * jax.random.uniform(seeds[3], (TOKENS, TOP), jnp.float32) ** block_levels(seeds[3], (TOKENS, TOP), ((0, 256),), -0.2, 0.2)), 0.05, 0.5)
    gate_weight = scatter_about(seeds[4], (EXPERTS, D, HID), D ** -0.5, 0.125, ((0, 32),))
    up_weight = scatter_about(seeds[5], (EXPERTS, D, HID), D ** -0.5, 0.125, ((0, 32),))
    down_weight = scatter_about(seeds[6], (EXPERTS, HID, D), HID ** -0.5, 0.3125, ((0, 32),))
    return dict(tokens=tokens, out_grad=out_grad, expert_ids=expert_ids, route_probs=route_probs, gate_weight=gate_weight, up_weight=up_weight, down_weight=down_weight)


def reference(tokens, out_grad, expert_ids, route_probs, gate_weight, up_weight, down_weight):
    blocks = N_DP * N_EXPERT
    pairs = TOK_DEV * TOP
    flat = expert_ids.reshape(blocks, pairs)
    columns = jnp.arange(EXPERTS, dtype=jnp.int32)
    onehot = (flat[:, :, None] == columns[None, None, :]).astype(jnp.int32)
    rank = jnp.sum(jnp.cumsum(onehot, axis=1) * onehot, axis=2) - 1
    slot = (flat * CAP + rank).astype(jnp.int32)
    block_ids = jnp.arange(blocks, dtype=jnp.int32)[:, None]
    local_ids = jnp.broadcast_to(jnp.arange(pairs, dtype=jnp.int32)[None, :], (blocks, pairs))
    table = jnp.full((blocks, EXPERTS * CAP), pairs, dtype=jnp.int32)
    table = table.at[jnp.broadcast_to(block_ids, (blocks, pairs)), slot].set(local_ids)
    glob = jnp.where(table < pairs, table + block_ids * pairs, blocks * pairs).astype(jnp.int32)
    table_e = glob.reshape(blocks, EXPERTS, CAP).transpose(1, 0, 2).reshape(EXPERTS, blocks * CAP)
    zero_row = jnp.zeros((1, D), dtype=jnp.bfloat16)
    x_pad = jnp.concatenate([tokens, zero_row], axis=0)
    dy_pad = jnp.concatenate([out_grad, zero_row], axis=0)
    p_pad = jnp.concatenate([route_probs.reshape(-1), jnp.zeros((1,), dtype=jnp.float32)], axis=0)

    def group_sum(left, right):
        lf = left.astype(jnp.float32).reshape(N_DP, N_EXPERT * CAP, left.shape[1])
        rf = right.astype(jnp.float32).reshape(N_DP, N_EXPERT * CAP, right.shape[1])
        parts = jnp.einsum("prd,prh->pdh", lf, rf).astype(jnp.bfloat16)
        return jnp.sum(parts.astype(jnp.float32), axis=0).astype(jnp.bfloat16)

    def one_expert(carry, inputs):
        rows, w_gate, w_up, w_down = inputs
        tok = (rows // TOP).astype(jnp.int32)
        xr = x_pad[tok]
        scaled = (p_pad[rows][:, None] * dy_pad[tok].astype(jnp.float32)).astype(jnp.bfloat16)
        gate = jnp.dot(xr, w_gate, preferred_element_type=jnp.float32)
        up = jnp.dot(xr, w_up, preferred_element_type=jnp.float32)
        sig = jax.nn.sigmoid(gate)
        act = (gate * sig * up).astype(jnp.bfloat16)
        dh = jnp.dot(scaled, w_down.T, preferred_element_type=jnp.float32)
        dgate = (dh * up * sig * (1.0 + gate * (1.0 - sig))).astype(jnp.bfloat16)
        dup = (dh * gate * sig).astype(jnp.bfloat16)
        contrib = (jnp.dot(dgate, w_gate.T, preferred_element_type=jnp.float32)
                   + jnp.dot(dup, w_up.T, preferred_element_type=jnp.float32)).astype(jnp.bfloat16)
        carry = carry.at[tok].add(contrib.astype(jnp.float32))
        grad_g = group_sum(xr, dgate)
        grad_u = group_sum(xr, dup)
        grad_d = group_sum(act, scaled)
        return carry, (grad_g, grad_u, grad_d)

    start = jnp.zeros((TOKENS + 1, D), dtype=jnp.float32)
    total, grads = lax.scan(one_expert, start, (table_e, gate_weight, up_weight, down_weight))
    in_grad = total[:TOKENS].astype(jnp.bfloat16)
    return (in_grad, grads[0], grads[1], grads[2])
```

```python
import jax
import jax.numpy as jnp
from jax import lax
from jax.sharding import PartitionSpec as P


def contract(left, right, left_dims, right_dims):
    return lax.dot_general(
        left, right, ((left_dims, right_dims), ((), ())), preferred_element_type=jnp.float32
    )


def dp_ring(n_dp):
    half = n_dp // 2
    return [2 * i for i in range(half)] + [2 * (half - 1 - i) + 1 for i in range(half)]


def ring_reduce_scatter(packed, n_dp):
    ring = dp_ring(n_dp)
    pos_of = [ring.index(d) for d in range(n_dp)]
    ring_arr = jnp.array(ring, dtype=jnp.int32)
    pos = jnp.array(pos_of, dtype=jnp.int32)[lax.axis_index("dp")]
    k = packed.shape[1] // 2
    halves = (packed[:, :k], packed[:, k:])
    steps = (1, -1)
    perms = [
        [(ring[i], ring[(i + st) % n_dp]) for i in range(n_dp)] for st in steps
    ]

    def own(h, c):
        return lax.dynamic_index_in_dim(halves[h], ring_arr[c % n_dp], axis=0, keepdims=False)

    send = [own(h, pos - steps[h]) for h in range(2)]
    acc = [None, None]
    for s in range(n_dp - 1):
        for h in range(2):
            recv = lax.ppermute(send[h], "dp", perms[h])
            chunk = pos - steps[h] * (s + 2)
            acc[h] = recv.astype(jnp.float32) + own(h, chunk).astype(jnp.float32)
            send[h] = acc[h].astype(jnp.bfloat16)
    return jnp.concatenate([send[0], send[1]], axis=0)


def expert_work(xr, scaled, w_gate, w_up, w_down):
    gate = contract(xr, w_gate, (1,), (0,))
    up = contract(xr, w_up, (1,), (0,))
    sig = jax.nn.sigmoid(gate)
    act = (gate * sig * up).astype(jnp.bfloat16)
    dh = contract(scaled, w_down, (1,), (1,))
    dgate = (dh * up * sig * (1.0 + gate * (1.0 - sig))).astype(jnp.bfloat16)
    dup = (dh * gate * sig).astype(jnp.bfloat16)
    contrib = (contract(dgate, w_gate, (1,), (1,)) + contract(dup, w_up, (1,), (1,))).astype(
        jnp.bfloat16
    )
    grad_g = contract(xr, dgate, (0,), (0,)).astype(jnp.bfloat16)
    grad_u = contract(xr, dup, (0,), (0,)).astype(jnp.bfloat16)
    grad_d = contract(act, scaled, (0,), (0,)).astype(jnp.bfloat16)
    return contrib, grad_g, grad_u, grad_d


def per_device(tokens, out_grad, expert_ids, route_probs, gate_weight, up_weight, down_weight):
    tok_dev, width = tokens.shape
    top_k = expert_ids.shape[1]
    exp_dev, _, hid = gate_weight.shape
    n_owner = lax.axis_size("expert")
    n_dp = lax.axis_size("dp")
    experts = exp_dev * n_owner
    slots = tok_dev * top_k * 9 // (experts * 8)
    n_slot = experts * slots
    rows = n_owner * slots

    columns = jnp.arange(experts, dtype=jnp.int32)
    onehot = expert_ids[:, :, None] == columns[None, None, :]
    per_tok = jnp.sum(onehot.astype(jnp.float32), axis=1).astype(jnp.bfloat16)
    t_ids = jnp.arange(tok_dev, dtype=jnp.int32)
    lower = (t_ids[None, :] < t_ids[:, None]).astype(jnp.bfloat16)
    before = contract(lower, per_tok, (1,), (0,))
    rank_prev = jnp.sum(jnp.where(onehot, before[:, None, :], 0.0), axis=2).astype(jnp.int32)
    k_ids = jnp.arange(top_k, dtype=jnp.int32)
    same = (expert_ids[:, :, None] == expert_ids[:, None, :]) & (k_ids[None, None, :] < k_ids[None, :, None])
    rank = rank_prev + jnp.sum(same.astype(jnp.int32), axis=2)
    dest = expert_ids * slots + rank

    s_ids = jnp.arange(n_slot, dtype=jnp.int32)
    hit = s_ids[:, None, None] == dest[None, :, :]
    sel = jnp.any(hit, axis=2).astype(jnp.bfloat16)
    p_slot = jnp.sum(jnp.where(hit, route_probs[None, :, :], 0.0), axis=(1, 2))
    sel = sel.reshape(n_owner, exp_dev, slots, tok_dev)
    p_slot = p_slot.reshape(n_owner, exp_dev, slots)

    contrib_back = []
    grads = []
    for local in range(exp_dev):
        sel_l = sel[:, local]
        send_x = contract(sel_l, tokens, (2,), (0,)).astype(jnp.bfloat16)
        dy_rows = contract(sel_l, out_grad, (2,), (0,))
        send_dy = (p_slot[:, local][:, :, None] * dy_rows).astype(jnp.bfloat16)
        send = jnp.concatenate([send_x, send_dy], axis=1)
        recv = lax.all_to_all(send, "expert", split_axis=0, concat_axis=0, tiled=True)
        xr = recv[:, :slots].reshape(rows, width)
        scaled = recv[:, slots:].reshape(rows, width)
        contrib, grad_g, grad_u, grad_d = expert_work(
            xr, scaled, gate_weight[local], up_weight[local], down_weight[local]
        )
        back = lax.all_to_all(
            contrib.reshape(n_owner, slots, width), "expert", split_axis=0, concat_axis=0, tiled=True
        )
        contrib_back.append(back)
        grads.append((grad_g, grad_u, grad_d))

    in_grad = None
    for local in range(exp_dev):
        part = contract(sel[:, local], contrib_back[local], (0, 1), (0, 1))
        in_grad = part if in_grad is None else in_grad + part
    in_grad = in_grad.astype(jnp.bfloat16)

    dsl = width // n_dp
    reduced = []
    for grad_g, grad_u, grad_d in grads:
        packed = jnp.concatenate(
            [
                grad_g.reshape(n_dp, dsl * hid),
                grad_u.reshape(n_dp, dsl * hid),
                grad_d.reshape(hid, n_dp, dsl).transpose(1, 0, 2).reshape(n_dp, hid * dsl),
            ],
            axis=1,
        )
        reduced.append(ring_reduce_scatter(packed, n_dp))
    stack_g = jnp.stack([r[: dsl * hid].reshape(dsl, hid) for r in reduced], axis=0)
    stack_u = jnp.stack([r[dsl * hid : 2 * dsl * hid].reshape(dsl, hid) for r in reduced], axis=0)
    stack_d = jnp.stack([r[2 * dsl * hid :].reshape(hid, dsl) for r in reduced], axis=0)
    return (in_grad, stack_g, stack_u, stack_d)


def solution(mesh):
    in_specs = (
        P(("dp", "expert"), None),
        P(("dp", "expert"), None),
        P(("dp", "expert"), None),
        P(("dp", "expert"), None),
        P("expert", None, None),
        P("expert", None, None),
        P("expert", None, None),
    )
    out_specs = (
        P(("dp", "expert"), None),
        P("expert", "dp", None),
        P("expert", "dp", None),
        P("expert", None, "dp"),
    )
    return jax.shard_map(
        per_device, mesh=mesh, in_specs=in_specs, out_specs=out_specs, check_vma=False
    )
```

```python
import jax
import jax.numpy as jnp
from jax import lax
from jax.sharding import PartitionSpec as P


def contract(left, right, left_dims, right_dims):
    return lax.dot_general(
        left, right, ((left_dims, right_dims), ((), ())), preferred_element_type=jnp.float32
    )


def dp_ring(n_dp):
    half = n_dp // 2
    return [2 * i for i in range(half)] + [2 * (half - 1 - i) + 1 for i in range(half)]


def ring_reduce_scatter(packed, n_dp):
    ring = dp_ring(n_dp)
    pos_of = [ring.index(d) for d in range(n_dp)]
    ring_arr = jnp.array(ring, dtype=jnp.int32)
    pos = jnp.array(pos_of, dtype=jnp.int32)[lax.axis_index("dp")]
    k = packed.shape[1] // 2
    halves = (packed[:, :k], packed[:, k:])
    steps = (1, -1)
    perms = [
        [(ring[i], ring[(i + st) % n_dp]) for i in range(n_dp)] for st in steps
    ]

    def own(h, c):
        return lax.dynamic_index_in_dim(halves[h], ring_arr[c % n_dp], axis=0, keepdims=False)

    send = [own(h, pos - steps[h]) for h in range(2)]
    acc = [None, None]
    for s in range(n_dp - 1):
        for h in range(2):
            recv = lax.ppermute(send[h], "dp", perms[h])
            chunk = pos - steps[h] * (s + 2)
            acc[h] = recv.astype(jnp.float32) + own(h, chunk).astype(jnp.float32)
            send[h] = acc[h].astype(jnp.bfloat16)
    return jnp.concatenate([send[0], send[1]], axis=0)


def expert_work(xr, scaled, w_gate, w_up, w_down):
    gate = contract(xr, w_gate, (2,), (0,))
    up = contract(xr, w_up, (2,), (0,))
    sig = jax.nn.sigmoid(gate)
    act = (gate * sig * up).astype(jnp.bfloat16)
    dh = contract(scaled, w_down, (2,), (1,))
    dgate = (dh * up * sig * (1.0 + gate * (1.0 - sig))).astype(jnp.bfloat16)
    dup = (dh * gate * sig).astype(jnp.bfloat16)
    contrib = (contract(dgate, w_gate, (2,), (1,)) + contract(dup, w_up, (2,), (1,))).astype(
        jnp.bfloat16
    )
    grad_g = contract(xr, dgate, (0, 1), (0, 1)).astype(jnp.bfloat16)
    grad_u = contract(xr, dup, (0, 1), (0, 1)).astype(jnp.bfloat16)
    grad_d = contract(act, scaled, (0, 1), (0, 1)).astype(jnp.bfloat16)
    return contrib, grad_g, grad_u, grad_d


def per_device(tokens, out_grad, expert_ids, route_probs, gate_weight, up_weight, down_weight):
    tok_dev, width = tokens.shape
    top_k = expert_ids.shape[1]
    exp_dev, _, hid = gate_weight.shape
    n_owner = lax.axis_size("expert")
    n_dp = lax.axis_size("dp")
    experts = exp_dev * n_owner
    slots = tok_dev * top_k * 9 // (experts * 8)
    n_slot = experts * slots

    columns = jnp.arange(experts, dtype=jnp.int32)
    onehot = expert_ids[:, :, None] == columns[None, None, :]
    per_tok = jnp.sum(onehot.astype(jnp.float32), axis=1).astype(jnp.bfloat16)
    t_ids = jnp.arange(tok_dev, dtype=jnp.int32)
    lower = (t_ids[None, :] < t_ids[:, None]).astype(jnp.bfloat16)
    before = contract(lower, per_tok, (1,), (0,))
    rank_prev = jnp.sum(jnp.where(onehot, before[:, None, :], 0.0), axis=2).astype(jnp.int32)
    k_ids = jnp.arange(top_k, dtype=jnp.int32)
    same = (expert_ids[:, :, None] == expert_ids[:, None, :]) & (k_ids[None, None, :] < k_ids[None, :, None])
    rank = rank_prev + jnp.sum(same.astype(jnp.int32), axis=2)
    dest = expert_ids * slots + rank

    s_ids = jnp.arange(n_slot, dtype=jnp.int32)
    hit = s_ids[:, None, None] == dest[None, :, :]
    sel = jnp.any(hit, axis=2).astype(jnp.bfloat16)
    p_slot = jnp.sum(jnp.where(hit, route_probs[None, :, :], 0.0), axis=(1, 2))
    sel = sel.reshape(n_owner, exp_dev, slots, tok_dev)
    p_slot = p_slot.reshape(n_owner, exp_dev, slots)

    contrib_back = []
    grads = []
    for local in range(exp_dev):
        sel_l = sel[:, local]
        send_x = contract(sel_l, tokens, (2,), (0,)).astype(jnp.bfloat16)
        dy_rows = contract(sel_l, out_grad, (2,), (0,))
        send_dy = (p_slot[:, local][:, :, None] * dy_rows).astype(jnp.bfloat16)
        send = jnp.concatenate([send_x, send_dy], axis=1)
        recv = lax.all_to_all(send, "expert", split_axis=0, concat_axis=0, tiled=True)
        xr = recv[:, :slots]
        scaled = recv[:, slots:]
        contrib, grad_g, grad_u, grad_d = expert_work(
            xr, scaled, gate_weight[local], up_weight[local], down_weight[local]
        )
        back = lax.all_to_all(contrib, "expert", split_axis=0, concat_axis=0, tiled=True)
        contrib_back.append(back)
        grads.append((grad_g, grad_u, grad_d))

    in_grad = None
    for local in range(exp_dev):
        part = contract(sel[:, local], contrib_back[local], (0, 1), (0, 1))
        in_grad = part if in_grad is None else in_grad + part
    in_grad = in_grad.astype(jnp.bfloat16)

    dsl = width // n_dp
    reduced = []
    for grad_g, grad_u, grad_d in grads:
        lanes = 1024
        packed = jnp.concatenate(
            [
                grad_g.reshape(n_dp, dsl * hid // lanes, lanes),
                grad_u.reshape(n_dp, dsl * hid // lanes, lanes),
                grad_d.reshape(hid, n_dp, dsl).transpose(1, 0, 2).reshape(n_dp, hid * dsl // lanes, lanes),
            ],
            axis=1,
        )
        reduced.append(ring_reduce_scatter(packed, n_dp).reshape(3, dsl * hid))
    stack_g = jnp.stack([r[0].reshape(dsl, hid) for r in reduced], axis=0)
    stack_u = jnp.stack([r[1].reshape(dsl, hid) for r in reduced], axis=0)
    stack_d = jnp.stack([r[2].reshape(hid, dsl) for r in reduced], axis=0)
    return (in_grad, stack_g, stack_u, stack_d)


def solution(mesh):
    in_specs = (
        P(("dp", "expert"), None),
        P(("dp", "expert"), None),
        P(("dp", "expert"), None),
        P(("dp", "expert"), None),
        P("expert", None, None),
        P("expert", None, None),
        P("expert", None, None),
    )
    out_specs = (
        P(("dp", "expert"), None),
        P("expert", "dp", None),
        P("expert", "dp", None),
        P("expert", None, "dp"),
    )
    return jax.shard_map(
        per_device, mesh=mesh, in_specs=in_specs, out_specs=out_specs, check_vma=False
    )
```

```python
import jax
import jax.numpy as jnp
from jax import lax
from jax.sharding import PartitionSpec as P


def contract(left, right, left_dims, right_dims):
    return lax.dot_general(
        left, right, ((left_dims, right_dims), ((), ())), preferred_element_type=jnp.float32
    )


def dp_ring(n_dp):
    half = n_dp // 2
    return [2 * i for i in range(half)] + [2 * (half - 1 - i) + 1 for i in range(half)]


def ring_reduce_scatter(packed, n_dp):
    ring = dp_ring(n_dp)
    pos_of = [ring.index(d) for d in range(n_dp)]
    ring_arr = jnp.array(ring, dtype=jnp.int32)
    pos = jnp.array(pos_of, dtype=jnp.int32)[lax.axis_index("dp")]
    k = packed.shape[1] // 2
    halves = (packed[:, :k], packed[:, k:])
    steps = (1, -1)
    perms = [
        [(ring[i], ring[(i + st) % n_dp]) for i in range(n_dp)] for st in steps
    ]

    def own(h, c):
        return lax.dynamic_index_in_dim(halves[h], ring_arr[c % n_dp], axis=0, keepdims=False)

    send = [own(h, pos - steps[h]) for h in range(2)]
    acc = [None, None]
    for s in range(n_dp - 1):
        for h in range(2):
            recv = lax.ppermute(send[h], "dp", perms[h])
            chunk = pos - steps[h] * (s + 2)
            acc[h] = recv.astype(jnp.float32) + own(h, chunk).astype(jnp.float32)
            send[h] = acc[h].astype(jnp.bfloat16)
    return jnp.concatenate([send[0], send[1]], axis=0)


def expert_work(xr, scaled, w_gate, w_up, w_down):
    gate = contract(xr, w_gate, (2,), (0,))
    up = contract(xr, w_up, (2,), (0,))
    sig = jax.nn.sigmoid(gate)
    act = (gate * sig * up).astype(jnp.bfloat16)
    dh = contract(scaled, w_down, (2,), (1,))
    dgate = (dh * up * sig * (1.0 + gate * (1.0 - sig))).astype(jnp.bfloat16)
    dup = (dh * gate * sig).astype(jnp.bfloat16)
    contrib = (contract(dgate, w_gate, (2,), (1,)) + contract(dup, w_up, (2,), (1,))).astype(
        jnp.bfloat16
    )
    grad_g = contract(xr, dgate, (0, 1), (0, 1)).astype(jnp.bfloat16)
    grad_u = contract(xr, dup, (0, 1), (0, 1)).astype(jnp.bfloat16)
    grad_d = contract(act, scaled, (0, 1), (0, 1)).astype(jnp.bfloat16)
    return contrib, grad_g, grad_u, grad_d


def per_device(tokens, out_grad, expert_ids, route_probs, gate_weight, up_weight, down_weight):
    tok_dev, width = tokens.shape
    top_k = expert_ids.shape[1]
    exp_dev, _, hid = gate_weight.shape
    n_owner = lax.axis_size("expert")
    n_dp = lax.axis_size("dp")
    experts = exp_dev * n_owner
    slots = tok_dev * top_k * 9 // (experts * 8)
    n_slot = experts * slots

    columns = jnp.arange(experts, dtype=jnp.int32)
    onehot = expert_ids[:, :, None] == columns[None, None, :]
    per_tok = jnp.sum(onehot.astype(jnp.float32), axis=1).astype(jnp.bfloat16)
    t_ids = jnp.arange(tok_dev, dtype=jnp.int32)
    lower = (t_ids[None, :] < t_ids[:, None]).astype(jnp.bfloat16)
    before = contract(lower, per_tok, (1,), (0,))
    rank_prev = jnp.sum(jnp.where(onehot, before[:, None, :], 0.0), axis=2).astype(jnp.int32)
    k_ids = jnp.arange(top_k, dtype=jnp.int32)
    same = (expert_ids[:, :, None] == expert_ids[:, None, :]) & (k_ids[None, None, :] < k_ids[None, :, None])
    rank = rank_prev + jnp.sum(same.astype(jnp.int32), axis=2)
    dest = expert_ids * slots + rank

    s_ids = jnp.arange(n_slot, dtype=jnp.int32)
    hit = s_ids[:, None, None] == dest[None, :, :]
    sel = jnp.any(hit, axis=2).astype(jnp.bfloat16)
    p_slot = jnp.sum(jnp.where(hit, route_probs[None, :, :], 0.0), axis=(1, 2))
    sel = sel.reshape(n_owner, exp_dev, slots, tok_dev)
    p_slot = p_slot.reshape(n_owner, exp_dev, slots)

    contribs = []
    grads = []
    for local in range(exp_dev):
        sel_l = sel[:, local]
        send_x = contract(sel_l, tokens, (2,), (0,)).astype(jnp.bfloat16)
        dy_rows = contract(sel_l, out_grad, (2,), (0,))
        send_dy = (p_slot[:, local][:, :, None] * dy_rows).astype(jnp.bfloat16)
        send = jnp.concatenate([send_x, send_dy], axis=1)
        recv = lax.all_to_all(send, "expert", split_axis=0, concat_axis=0, tiled=True)
        xr = recv[:, :slots]
        scaled = recv[:, slots:]
        contrib, grad_g, grad_u, grad_d = expert_work(
            xr, scaled, gate_weight[local], up_weight[local], down_weight[local]
        )
        contribs.append(contrib)
        grads.append((grad_g, grad_u, grad_d))

    back = lax.all_to_all(
        jnp.concatenate(contribs, axis=1), "expert", split_axis=0, concat_axis=0, tiled=True
    )
    sel_all = sel.reshape(n_owner, exp_dev * slots, tok_dev)
    in_grad = contract(sel_all, back, (0, 1), (0, 1)).astype(jnp.bfloat16)

    dsl = width // n_dp
    reduced = []
    for grad_g, grad_u, grad_d in grads:
        lanes = 1024
        packed = jnp.concatenate(
            [
                grad_g.reshape(n_dp, dsl * hid // lanes, lanes),
                grad_u.reshape(n_dp, dsl * hid // lanes, lanes),
                grad_d.reshape(hid, n_dp, dsl).transpose(1, 0, 2).reshape(n_dp, hid * dsl // lanes, lanes),
            ],
            axis=1,
        )
        reduced.append(ring_reduce_scatter(packed, n_dp).reshape(3, dsl * hid))
    stack_g = jnp.stack([r[0].reshape(dsl, hid) for r in reduced], axis=0)
    stack_u = jnp.stack([r[1].reshape(dsl, hid) for r in reduced], axis=0)
    stack_d = jnp.stack([r[2].reshape(hid, dsl) for r in reduced], axis=0)
    return (in_grad, stack_g, stack_u, stack_d)


def solution(mesh):
    in_specs = (
        P(("dp", "expert"), None),
        P(("dp", "expert"), None),
        P(("dp", "expert"), None),
        P(("dp", "expert"), None),
        P("expert", None, None),
        P("expert", None, None),
        P("expert", None, None),
    )
    out_specs = (
        P(("dp", "expert"), None),
        P("expert", "dp", None),
        P("expert", "dp", None),
        P("expert", None, "dp"),
    )
    return jax.shard_map(
        per_device, mesh=mesh, in_specs=in_specs, out_specs=out_specs, check_vma=False
    )
```

```python
import jax
import jax.numpy as jnp
from jax import lax
from jax.sharding import PartitionSpec as P


def contract(left, right, left_dims, right_dims):
    return lax.dot_general(
        left, right, ((left_dims, right_dims), ((), ())), preferred_element_type=jnp.float32
    )


def dp_reduce_scatter(packed, n_dp):
    n_y = n_dp // 2
    _, n_r, lanes = packed.shape
    me = lax.axis_index("dp")
    y_pos = me // 2
    x_lo = me % 2
    by_y = packed.reshape(n_y, 2, n_r, lanes)
    half = n_r // 2
    halves = (by_y[:, :, :half], by_y[:, :, half:])
    steps = (1, -1)
    perms = [
        [(y * 2 + b, ((y + st) % n_y) * 2 + b) for y in range(n_y) for b in range(2)]
        for st in steps
    ]

    def own(h, c):
        return lax.dynamic_index_in_dim(halves[h], c % n_y, axis=0, keepdims=False)

    send = [own(h, y_pos - steps[h]) for h in range(2)]
    for s in range(n_y - 1):
        for h in range(2):
            recv = lax.ppermute(send[h], "dp", perms[h])
            chunk = y_pos - steps[h] * (s + 2)
            acc = recv.astype(jnp.float32) + own(h, chunk).astype(jnp.float32)
            send[h] = acc.astype(jnp.bfloat16)
    both = jnp.concatenate(send, axis=1)
    keep = lax.dynamic_index_in_dim(both, x_lo, axis=0, keepdims=False)
    give = lax.dynamic_index_in_dim(both, 1 - x_lo, axis=0, keepdims=False)
    got = lax.ppermute(give, "dp", [(d, d ^ 1) for d in range(n_dp)])
    return (keep.astype(jnp.float32) + got.astype(jnp.float32)).astype(jnp.bfloat16)


def expert_work(xr, scaled, w_gate, w_up, w_down):
    gate = contract(xr, w_gate, (2,), (0,))
    up = contract(xr, w_up, (2,), (0,))
    sig = jax.nn.sigmoid(gate)
    act = (gate * sig * up).astype(jnp.bfloat16)
    dh = contract(scaled, w_down, (2,), (1,))
    dgate = (dh * up * sig * (1.0 + gate * (1.0 - sig))).astype(jnp.bfloat16)
    dup = (dh * gate * sig).astype(jnp.bfloat16)
    contrib = (contract(dgate, w_gate, (2,), (1,)) + contract(dup, w_up, (2,), (1,))).astype(
        jnp.bfloat16
    )
    grad_g = contract(xr, dgate, (0, 1), (0, 1)).astype(jnp.bfloat16)
    grad_u = contract(xr, dup, (0, 1), (0, 1)).astype(jnp.bfloat16)
    grad_d = contract(act, scaled, (0, 1), (0, 1)).astype(jnp.bfloat16)
    return contrib, grad_g, grad_u, grad_d


def per_device(tokens, out_grad, expert_ids, route_probs, gate_weight, up_weight, down_weight):
    tok_dev, width = tokens.shape
    top_k = expert_ids.shape[1]
    exp_dev, _, hid = gate_weight.shape
    n_owner = lax.axis_size("expert")
    n_dp = lax.axis_size("dp")
    experts = exp_dev * n_owner
    slots = tok_dev * top_k * 9 // (experts * 8)
    n_slot = experts * slots

    columns = jnp.arange(experts, dtype=jnp.int32)
    onehot = expert_ids[:, :, None] == columns[None, None, :]
    per_tok = jnp.sum(onehot.astype(jnp.float32), axis=1).astype(jnp.bfloat16)
    t_ids = jnp.arange(tok_dev, dtype=jnp.int32)
    lower = (t_ids[None, :] < t_ids[:, None]).astype(jnp.bfloat16)
    before = contract(lower, per_tok, (1,), (0,))
    rank_prev = jnp.sum(jnp.where(onehot, before[:, None, :], 0.0), axis=2).astype(jnp.int32)
    k_ids = jnp.arange(top_k, dtype=jnp.int32)
    same = (expert_ids[:, :, None] == expert_ids[:, None, :]) & (k_ids[None, None, :] < k_ids[None, :, None])
    rank = rank_prev + jnp.sum(same.astype(jnp.int32), axis=2)
    dest = expert_ids * slots + rank

    s_ids = jnp.arange(n_slot, dtype=jnp.int32)
    hit = s_ids[:, None, None] == dest[None, :, :]
    sel = jnp.any(hit, axis=2).astype(jnp.bfloat16)
    p_slot = jnp.sum(jnp.where(hit, route_probs[None, :, :], 0.0), axis=(1, 2))
    sel = sel.reshape(n_owner, exp_dev, slots, tok_dev)
    p_slot = p_slot.reshape(n_owner, exp_dev, slots)

    contribs = []
    grads = []
    for local in range(exp_dev):
        sel_l = sel[:, local]
        send_x = contract(sel_l, tokens, (2,), (0,)).astype(jnp.bfloat16)
        dy_rows = contract(sel_l, out_grad, (2,), (0,))
        send_dy = (p_slot[:, local][:, :, None] * dy_rows).astype(jnp.bfloat16)
        send = jnp.concatenate([send_x, send_dy], axis=1)
        recv = lax.all_to_all(send, "expert", split_axis=0, concat_axis=0, tiled=True)
        xr = recv[:, :slots]
        scaled = recv[:, slots:]
        contrib, grad_g, grad_u, grad_d = expert_work(
            xr, scaled, gate_weight[local], up_weight[local], down_weight[local]
        )
        contribs.append(contrib)
        grads.append((grad_g, grad_u, grad_d))

    back = lax.all_to_all(
        jnp.concatenate(contribs, axis=1), "expert", split_axis=0, concat_axis=0, tiled=True
    )
    sel_all = sel.reshape(n_owner, exp_dev * slots, tok_dev)
    in_grad = contract(sel_all, back, (0, 1), (0, 1)).astype(jnp.bfloat16)

    dsl = width // n_dp
    reduced = []
    for grad_g, grad_u, grad_d in grads:
        lanes = 1024
        packed = jnp.concatenate(
            [
                grad_g.reshape(n_dp, dsl * hid // lanes, lanes),
                grad_u.reshape(n_dp, dsl * hid // lanes, lanes),
                grad_d.reshape(hid, n_dp, dsl).transpose(1, 0, 2).reshape(n_dp, hid * dsl // lanes, lanes),
            ],
            axis=1,
        )
        reduced.append(dp_reduce_scatter(packed, n_dp).reshape(3, dsl * hid))
    stack_g = jnp.stack([r[0].reshape(dsl, hid) for r in reduced], axis=0)
    stack_u = jnp.stack([r[1].reshape(dsl, hid) for r in reduced], axis=0)
    stack_d = jnp.stack([r[2].reshape(hid, dsl) for r in reduced], axis=0)
    return (in_grad, stack_g, stack_u, stack_d)


def solution(mesh):
    in_specs = (
        P(("dp", "expert"), None),
        P(("dp", "expert"), None),
        P(("dp", "expert"), None),
        P(("dp", "expert"), None),
        P("expert", None, None),
        P("expert", None, None),
        P("expert", None, None),
    )
    out_specs = (
        P(("dp", "expert"), None),
        P("expert", "dp", None),
        P("expert", "dp", None),
        P("expert", None, "dp"),
    )
    return jax.shard_map(
        per_device, mesh=mesh, in_specs=in_specs, out_specs=out_specs, check_vma=False
    )
```

```python
import jax
import jax.numpy as jnp
from jax import lax
from jax.sharding import PartitionSpec as P


def contract(left, right, left_dims, right_dims):
    return lax.dot_general(
        left, right, ((left_dims, right_dims), ((), ())), preferred_element_type=jnp.float32
    )


def dp_reduce_scatter(packed, n_dp):
    n_y = n_dp // 2
    _, n_r, lanes = packed.shape
    me = lax.axis_index("dp")
    y_pos = me // 2
    x_lo = me % 2
    by_y = packed.reshape(n_y, 2, n_r, lanes)
    half = n_r // 2
    halves = (by_y[:, :, :half], by_y[:, :, half:])
    steps = (1, -1)
    perms = [
        [(y * 2 + b, ((y + st) % n_y) * 2 + b) for y in range(n_y) for b in range(2)]
        for st in steps
    ]

    def own(h, c):
        return lax.dynamic_index_in_dim(halves[h], c % n_y, axis=0, keepdims=False)

    send = [own(h, y_pos - steps[h]) for h in range(2)]
    for s in range(n_y - 1):
        for h in range(2):
            recv = lax.ppermute(send[h], "dp", perms[h])
            chunk = y_pos - steps[h] * (s + 2)
            acc = recv.astype(jnp.float32) + own(h, chunk).astype(jnp.float32)
            send[h] = acc.astype(jnp.bfloat16)
    both = jnp.concatenate(send, axis=1)
    keep = lax.dynamic_index_in_dim(both, x_lo, axis=0, keepdims=False)
    give = lax.dynamic_index_in_dim(both, 1 - x_lo, axis=0, keepdims=False)
    got = lax.ppermute(give, "dp", [(d, d ^ 1) for d in range(n_dp)])
    return (keep.astype(jnp.float32) + got.astype(jnp.float32)).astype(jnp.bfloat16)


def expert_work(xr, scaled, w_gate, w_up, w_down):
    gate = contract(xr, w_gate, (2,), (0,))
    up = contract(xr, w_up, (2,), (0,))
    sig = jax.nn.sigmoid(gate)
    act = (gate * sig * up).astype(jnp.bfloat16)
    dh = contract(scaled, w_down, (2,), (1,))
    dgate = (dh * up * sig * (1.0 + gate * (1.0 - sig))).astype(jnp.bfloat16)
    dup = (dh * gate * sig).astype(jnp.bfloat16)
    contrib = (contract(dgate, w_gate, (2,), (1,)) + contract(dup, w_up, (2,), (1,))).astype(
        jnp.bfloat16
    )
    grad_g = contract(xr, dgate, (0, 1), (0, 1)).astype(jnp.bfloat16)
    grad_u = contract(xr, dup, (0, 1), (0, 1)).astype(jnp.bfloat16)
    grad_d = contract(act, scaled, (0, 1), (0, 1)).astype(jnp.bfloat16)
    return contrib, grad_g, grad_u, grad_d


def per_device(tokens, out_grad, expert_ids, route_probs, gate_weight, up_weight, down_weight):
    tok_dev, width = tokens.shape
    top_k = expert_ids.shape[1]
    exp_dev, _, hid = gate_weight.shape
    n_owner = lax.axis_size("expert")
    n_dp = lax.axis_size("dp")
    experts = exp_dev * n_owner
    slots = tok_dev * top_k * 9 // (experts * 8)
    n_slot = experts * slots

    columns = jnp.arange(experts, dtype=jnp.int32)
    onehot = expert_ids[:, :, None] == columns[None, None, :]
    member = jnp.any(onehot, axis=1)
    t_ids = jnp.arange(tok_dev, dtype=jnp.int32)
    lower = (t_ids[None, :] < t_ids[:, None]).astype(jnp.bfloat16)
    before = contract(member.astype(jnp.bfloat16), lower, (0,), (1,)).astype(jnp.int32)
    p_tok = jnp.sum(jnp.where(onehot, route_probs[:, :, None], 0.0), axis=1).T

    r_ids = jnp.arange(slots, dtype=jnp.int32)
    hit = member.T[:, None, :] & (before[:, None, :] == r_ids[None, :, None])
    p_slot = jnp.sum(jnp.where(hit, p_tok[:, None, :], 0.0), axis=2)
    sel = hit.astype(jnp.bfloat16).reshape(n_owner, exp_dev, slots, tok_dev)
    p_slot = p_slot.reshape(n_owner, exp_dev, slots)
    both_in = jnp.concatenate([tokens, out_grad], axis=0)
    zeros = jnp.zeros_like(sel[:, 0])
    ones = jnp.ones((n_owner, slots), jnp.float32)

    contribs = []
    grads = []
    after = None
    for local in range(exp_dev):
        sel_l = sel[:, local]
        pick = jnp.concatenate(
            [jnp.concatenate([sel_l, zeros], axis=2), jnp.concatenate([zeros, sel_l], axis=2)], axis=1
        )
        scale = jnp.concatenate([ones, p_slot[:, local]], axis=1)
        send = (scale[:, :, None] * contract(pick, both_in, (2,), (0,))).astype(jnp.bfloat16)
        recv = lax.all_to_all(send, "expert", split_axis=0, concat_axis=0, tiled=True)
        if after is not None:
            recv, _ = lax.optimization_barrier((recv, after))
        xr = recv[:, :slots]
        scaled = recv[:, slots:]
        contrib, grad_g, grad_u, grad_d = expert_work(
            xr, scaled, gate_weight[local], up_weight[local], down_weight[local]
        )
        after = contrib
        contribs.append(contrib)
        grads.append((grad_g, grad_u, grad_d))

    back = lax.all_to_all(
        jnp.concatenate(contribs, axis=1), "expert", split_axis=0, concat_axis=0, tiled=True
    )
    sel_all = sel.reshape(n_owner, exp_dev * slots, tok_dev)
    in_grad = contract(sel_all, back, (0, 1), (0, 1)).astype(jnp.bfloat16)

    dsl = width // n_dp
    reduced = []
    for grad_g, grad_u, grad_d in grads:
        lanes = 1024
        packed = jnp.concatenate(
            [
                grad_g.reshape(n_dp, dsl * hid // lanes, lanes),
                grad_u.reshape(n_dp, dsl * hid // lanes, lanes),
                grad_d.reshape(hid, n_dp, dsl).transpose(1, 0, 2).reshape(n_dp, hid * dsl // lanes, lanes),
            ],
            axis=1,
        )
        reduced.append(dp_reduce_scatter(packed, n_dp).reshape(3, dsl * hid))
    stack_g = jnp.stack([r[0].reshape(dsl, hid) for r in reduced], axis=0)
    stack_u = jnp.stack([r[1].reshape(dsl, hid) for r in reduced], axis=0)
    stack_d = jnp.stack([r[2].reshape(hid, dsl) for r in reduced], axis=0)
    return (in_grad, stack_g, stack_u, stack_d)


def solution(mesh):
    in_specs = (
        P(("dp", "expert"), None),
        P(("dp", "expert"), None),
        P(("dp", "expert"), None),
        P(("dp", "expert"), None),
        P("expert", None, None),
        P("expert", None, None),
        P("expert", None, None),
    )
    out_specs = (
        P(("dp", "expert"), None),
        P("expert", "dp", None),
        P("expert", "dp", None),
        P("expert", None, "dp"),
    )
    return jax.shard_map(
        per_device, mesh=mesh, in_specs=in_specs, out_specs=out_specs, check_vma=False
    )
```

```python
import jax
import jax.numpy as jnp
from jax import lax
from jax.sharding import PartitionSpec as P


def contract(left, right, left_dims, right_dims):
    return lax.dot_general(
        left, right, ((left_dims, right_dims), ((), ())), preferred_element_type=jnp.float32
    )


def dp_reduce_scatter(packed, n_dp):
    n_y = n_dp // 2
    _, n_r, lanes = packed.shape
    me = lax.axis_index("dp")
    y_pos = me // 2
    x_lo = me % 2
    by_y = packed.reshape(n_y, 2, n_r, lanes)
    half = n_r // 2
    halves = (by_y[:, :, :half], by_y[:, :, half:])
    steps = (1, -1)
    perms = [
        [(y * 2 + b, ((y + st) % n_y) * 2 + b) for y in range(n_y) for b in range(2)]
        for st in steps
    ]

    def own(h, c):
        return lax.dynamic_index_in_dim(halves[h], c % n_y, axis=0, keepdims=False)

    send = [own(h, y_pos - steps[h]) for h in range(2)]
    for s in range(n_y - 1):
        for h in range(2):
            recv = lax.ppermute(send[h], "dp", perms[h])
            chunk = y_pos - steps[h] * (s + 2)
            acc = recv.astype(jnp.float32) + own(h, chunk).astype(jnp.float32)
            send[h] = acc.astype(jnp.bfloat16)
    both = jnp.concatenate(send, axis=1)
    keep = lax.dynamic_index_in_dim(both, x_lo, axis=0, keepdims=False)
    give = lax.dynamic_index_in_dim(both, 1 - x_lo, axis=0, keepdims=False)
    got = lax.ppermute(give, "dp", [(d, d ^ 1) for d in range(n_dp)])
    return (keep.astype(jnp.float32) + got.astype(jnp.float32)).astype(jnp.bfloat16)


def pack_grads(grad_g, grad_u, grad_d, n_dp, lanes=1024):
    width, hid = grad_g.shape
    dsl = width // n_dp
    return jnp.concatenate(
        [
            grad_g.reshape(n_dp, dsl * hid // lanes, lanes),
            grad_u.reshape(n_dp, dsl * hid // lanes, lanes),
            grad_d.reshape(hid, n_dp, dsl).transpose(1, 0, 2).reshape(n_dp, hid * dsl // lanes, lanes),
        ],
        axis=1,
    )


def expert_work(xr, scaled, w_gate, w_up, w_down):
    gate = contract(xr, w_gate, (2,), (0,))
    up = contract(xr, w_up, (2,), (0,))
    sig = jax.nn.sigmoid(gate)
    act = (gate * sig * up).astype(jnp.bfloat16)
    dh = contract(scaled, w_down, (2,), (1,))
    dgate = (dh * up * sig * (1.0 + gate * (1.0 - sig))).astype(jnp.bfloat16)
    dup = (dh * gate * sig).astype(jnp.bfloat16)
    contrib = (contract(dgate, w_gate, (2,), (1,)) + contract(dup, w_up, (2,), (1,))).astype(
        jnp.bfloat16
    )
    grad_g = contract(xr, dgate, (0, 1), (0, 1)).astype(jnp.bfloat16)
    grad_u = contract(xr, dup, (0, 1), (0, 1)).astype(jnp.bfloat16)
    grad_d = contract(act, scaled, (0, 1), (0, 1)).astype(jnp.bfloat16)
    return contrib, grad_g, grad_u, grad_d


def per_device(tokens, out_grad, expert_ids, route_probs, gate_weight, up_weight, down_weight):
    tok_dev, width = tokens.shape
    top_k = expert_ids.shape[1]
    exp_dev, _, hid = gate_weight.shape
    n_owner = lax.axis_size("expert")
    n_dp = lax.axis_size("dp")
    experts = exp_dev * n_owner
    slots = tok_dev * top_k * 9 // (experts * 8)
    n_slot = experts * slots

    columns = jnp.arange(experts, dtype=jnp.int32)
    onehot = expert_ids[:, :, None] == columns[None, None, :]
    member = jnp.any(onehot, axis=1)
    t_ids = jnp.arange(tok_dev, dtype=jnp.int32)
    lower = (t_ids[None, :] < t_ids[:, None]).astype(jnp.bfloat16)
    before = contract(member.astype(jnp.bfloat16), lower, (0,), (1,)).astype(jnp.int32)
    p_tok = jnp.sum(jnp.where(onehot, route_probs[:, :, None], 0.0), axis=1).T

    r_ids = jnp.arange(slots, dtype=jnp.int32)
    hit = member.T[:, None, :] & (before[:, None, :] == r_ids[None, :, None])
    p_slot = jnp.sum(jnp.where(hit, p_tok[:, None, :], 0.0), axis=2)
    sel = hit.astype(jnp.bfloat16).reshape(n_owner, exp_dev, slots, tok_dev)
    p_slot = p_slot.reshape(n_owner, exp_dev, slots)
    both_in = jnp.concatenate([tokens, out_grad], axis=0)
    zeros = jnp.zeros_like(sel[:, 0])
    ones = jnp.ones((n_owner, slots), jnp.float32)

    contribs = []
    grads = []
    after = None
    for local in range(exp_dev):
        sel_l = sel[:, local]
        pick = jnp.concatenate(
            [jnp.concatenate([sel_l, zeros], axis=2), jnp.concatenate([zeros, sel_l], axis=2)], axis=1
        )
        scale = jnp.concatenate([ones, p_slot[:, local]], axis=1)
        send = (scale[:, :, None] * contract(pick, both_in, (2,), (0,))).astype(jnp.bfloat16)
        recv = lax.all_to_all(send, "expert", split_axis=0, concat_axis=0, tiled=True)
        if after is not None:
            recv, _ = lax.optimization_barrier((recv, after))
        xr = recv[:, :slots]
        scaled = recv[:, slots:]
        contrib, grad_g, grad_u, grad_d = expert_work(
            xr, scaled, gate_weight[local], up_weight[local], down_weight[local]
        )
        reduced = dp_reduce_scatter(pack_grads(grad_g, grad_u, grad_d, n_dp), n_dp)
        after = (contrib, reduced)
        contribs.append(contrib)
        grads.append(reduced.reshape(3, -1))

    back = lax.all_to_all(
        jnp.concatenate(contribs, axis=1), "expert", split_axis=0, concat_axis=0, tiled=True
    )
    sel_all = sel.reshape(n_owner, exp_dev * slots, tok_dev)
    in_grad = contract(sel_all, back, (0, 1), (0, 1)).astype(jnp.bfloat16)

    dsl = width // n_dp
    stack_g = jnp.stack([r[0].reshape(dsl, hid) for r in grads], axis=0)
    stack_u = jnp.stack([r[1].reshape(dsl, hid) for r in grads], axis=0)
    stack_d = jnp.stack([r[2].reshape(hid, dsl) for r in grads], axis=0)
    return (in_grad, stack_g, stack_u, stack_d)


def solution(mesh):
    in_specs = (
        P(("dp", "expert"), None),
        P(("dp", "expert"), None),
        P(("dp", "expert"), None),
        P(("dp", "expert"), None),
        P("expert", None, None),
        P("expert", None, None),
        P("expert", None, None),
    )
    out_specs = (
        P(("dp", "expert"), None),
        P("expert", "dp", None),
        P("expert", "dp", None),
        P("expert", None, "dp"),
    )
    return jax.shard_map(
        per_device, mesh=mesh, in_specs=in_specs, out_specs=out_specs, check_vma=False
    )
```

```python
import jax
import jax.numpy as jnp
from jax import lax
from jax.sharding import PartitionSpec as P


def contract(left, right, left_dims, right_dims):
    return lax.dot_general(
        left, right, ((left_dims, right_dims), ((), ())), preferred_element_type=jnp.float32
    )


def dp_reduce_scatter(packed, n_dp):
    n_y = n_dp // 2
    _, n_r, lanes = packed.shape
    me = lax.axis_index("dp")
    y_pos = me // 2
    x_lo = me % 2
    by_y = packed.reshape(n_y, 2, n_r, lanes)
    half = n_r // 2
    halves = (by_y[:, :, :half], by_y[:, :, half:])
    steps = (1, -1)
    perms = [
        [(y * 2 + b, ((y + st) % n_y) * 2 + b) for y in range(n_y) for b in range(2)]
        for st in steps
    ]

    def own(h, c):
        return lax.dynamic_index_in_dim(halves[h], c % n_y, axis=0, keepdims=False)

    send = [own(h, y_pos - steps[h]) for h in range(2)]
    for s in range(n_y - 1):
        for h in range(2):
            recv = lax.ppermute(send[h], "dp", perms[h])
            chunk = y_pos - steps[h] * (s + 2)
            acc = recv.astype(jnp.float32) + own(h, chunk).astype(jnp.float32)
            send[h] = acc.astype(jnp.bfloat16)
    both = jnp.concatenate(send, axis=1)
    keep = lax.dynamic_index_in_dim(both, x_lo, axis=0, keepdims=False)
    give = lax.dynamic_index_in_dim(both, 1 - x_lo, axis=0, keepdims=False)
    got = lax.ppermute(give, "dp", [(d, d ^ 1) for d in range(n_dp)])
    return (keep.astype(jnp.float32) + got.astype(jnp.float32)).astype(jnp.bfloat16)


def pack_grads(grad_g, grad_u, grad_d, n_dp, lanes=1024):
    width, hid = grad_g.shape
    dsl = width // n_dp
    return jnp.concatenate(
        [
            grad_g.reshape(n_dp, dsl * hid // lanes, lanes),
            grad_u.reshape(n_dp, dsl * hid // lanes, lanes),
            grad_d.reshape(hid, n_dp, dsl).transpose(1, 0, 2).reshape(n_dp, hid * dsl // lanes, lanes),
        ],
        axis=1,
    )


def expert_work(xr, scaled, w_gate_up, w_down):
    hid = w_down.shape[0]
    gate_up = contract(xr, w_gate_up, (2,), (0,))
    gate = gate_up[..., :hid]
    up = gate_up[..., hid:]
    sig = jax.nn.sigmoid(gate)
    act = (gate * sig * up).astype(jnp.bfloat16)
    dh = contract(scaled, w_down, (2,), (1,))
    dgate = (dh * up * sig * (1.0 + gate * (1.0 - sig))).astype(jnp.bfloat16)
    dup = (dh * gate * sig).astype(jnp.bfloat16)
    dboth = jnp.concatenate([dgate, dup], axis=2)
    contrib = contract(dboth, w_gate_up, (2,), (1,)).astype(jnp.bfloat16)
    grad_g = contract(xr, dgate, (0, 1), (0, 1)).astype(jnp.bfloat16)
    grad_u = contract(xr, dup, (0, 1), (0, 1)).astype(jnp.bfloat16)
    grad_d = contract(act, scaled, (0, 1), (0, 1)).astype(jnp.bfloat16)
    return contrib, grad_g, grad_u, grad_d


def per_device(tokens, out_grad, expert_ids, route_probs, gate_weight, up_weight, down_weight):
    tok_dev, width = tokens.shape
    top_k = expert_ids.shape[1]
    exp_dev, _, hid = gate_weight.shape
    n_owner = lax.axis_size("expert")
    n_dp = lax.axis_size("dp")
    experts = exp_dev * n_owner
    slots = tok_dev * top_k * 9 // (experts * 8)
    n_slot = experts * slots

    columns = jnp.arange(experts, dtype=jnp.int32)
    onehot = expert_ids[:, :, None] == columns[None, None, :]
    member = jnp.any(onehot, axis=1)
    t_ids = jnp.arange(tok_dev, dtype=jnp.int32)
    lower = (t_ids[None, :] < t_ids[:, None]).astype(jnp.bfloat16)
    before = contract(member.astype(jnp.bfloat16), lower, (0,), (1,)).astype(jnp.int32)
    p_tok = jnp.sum(jnp.where(onehot, route_probs[:, :, None], 0.0), axis=1).T

    r_ids = jnp.arange(slots, dtype=jnp.int32)
    hit = member.T[:, None, :] & (before[:, None, :] == r_ids[None, :, None])
    p_slot = jnp.sum(jnp.where(hit, p_tok[:, None, :], 0.0), axis=2)
    sel = hit.astype(jnp.bfloat16).reshape(n_owner, exp_dev, slots, tok_dev)
    p_slot = p_slot.reshape(n_owner, exp_dev, slots)
    both_in = jnp.concatenate([tokens, out_grad], axis=0)
    zeros = jnp.zeros_like(sel[:, 0])
    ones = jnp.ones((n_owner, slots), jnp.float32)

    w_gate_up = jnp.concatenate([gate_weight, up_weight], axis=2)
    contribs = []
    grads = []
    after = None
    for local in range(exp_dev):
        sel_l = sel[:, local]
        pick = jnp.concatenate(
            [jnp.concatenate([sel_l, zeros], axis=2), jnp.concatenate([zeros, sel_l], axis=2)], axis=1
        )
        scale = jnp.concatenate([ones, p_slot[:, local]], axis=1)
        send = (scale[:, :, None] * contract(pick, both_in, (2,), (0,))).astype(jnp.bfloat16)
        recv = lax.all_to_all(send, "expert", split_axis=0, concat_axis=0, tiled=True)
        if after is not None:
            recv, _ = lax.optimization_barrier((recv, after))
        xr = recv[:, :slots]
        scaled = recv[:, slots:]
        contrib, grad_g, grad_u, grad_d = expert_work(
            xr, scaled, w_gate_up[local], down_weight[local]
        )
        reduced = dp_reduce_scatter(pack_grads(grad_g, grad_u, grad_d, n_dp), n_dp)
        after = (contrib, reduced)
        contribs.append(contrib)
        grads.append(reduced.reshape(3, -1))

    back = lax.all_to_all(
        jnp.concatenate(contribs, axis=1), "expert", split_axis=0, concat_axis=0, tiled=True
    )
    sel_all = sel.reshape(n_owner, exp_dev * slots, tok_dev)
    in_grad = contract(sel_all, back, (0, 1), (0, 1)).astype(jnp.bfloat16)

    dsl = width // n_dp
    stack_g = jnp.stack([r[0].reshape(dsl, hid) for r in grads], axis=0)
    stack_u = jnp.stack([r[1].reshape(dsl, hid) for r in grads], axis=0)
    stack_d = jnp.stack([r[2].reshape(hid, dsl) for r in grads], axis=0)
    return (in_grad, stack_g, stack_u, stack_d)


def solution(mesh):
    in_specs = (
        P(("dp", "expert"), None),
        P(("dp", "expert"), None),
        P(("dp", "expert"), None),
        P(("dp", "expert"), None),
        P("expert", None, None),
        P("expert", None, None),
        P("expert", None, None),
    )
    out_specs = (
        P(("dp", "expert"), None),
        P("expert", "dp", None),
        P("expert", "dp", None),
        P("expert", None, "dp"),
    )
    return jax.shard_map(
        per_device, mesh=mesh, in_specs=in_specs, out_specs=out_specs, check_vma=False
    )
```

```python
import jax
import jax.numpy as jnp
from jax import lax
from jax.sharding import PartitionSpec as P


def contract(left, right, left_dims, right_dims):
    return lax.dot_general(
        left, right, ((left_dims, right_dims), ((), ())), preferred_element_type=jnp.float32
    )


def dp_reduce_scatter(packed, n_dp):
    n_y = n_dp // 2
    _, n_r, lanes = packed.shape
    me = lax.axis_index("dp")
    y_pos = me // 2
    x_lo = me % 2
    by_y = packed.reshape(n_y, 2, n_r, lanes)
    perm = [(y * 2 + b, ((y + 1) % n_y) * 2 + b) for y in range(n_y) for b in range(2)]

    def own(c):
        return lax.dynamic_index_in_dim(by_y, c % n_y, axis=0, keepdims=False)

    send = own(y_pos - 1)
    for s in range(n_y - 1):
        recv = lax.ppermute(send, "dp", perm)
        acc = recv.astype(jnp.float32) + own(y_pos - (s + 2)).astype(jnp.float32)
        send = acc.astype(jnp.bfloat16)
    both = send
    keep = lax.dynamic_index_in_dim(both, x_lo, axis=0, keepdims=False)
    give = lax.dynamic_index_in_dim(both, 1 - x_lo, axis=0, keepdims=False)
    got = lax.ppermute(give, "dp", [(d, d ^ 1) for d in range(n_dp)])
    return (keep.astype(jnp.float32) + got.astype(jnp.float32)).astype(jnp.bfloat16)


def pack_grads(grad_g, grad_u, grad_d, n_dp, lanes=1024):
    width, hid = grad_g.shape
    dsl = width // n_dp
    return jnp.concatenate(
        [
            grad_g.reshape(n_dp, dsl * hid // lanes, lanes),
            grad_u.reshape(n_dp, dsl * hid // lanes, lanes),
            grad_d.reshape(hid, n_dp, dsl).transpose(1, 0, 2).reshape(n_dp, hid * dsl // lanes, lanes),
        ],
        axis=1,
    )


def expert_work(xr, scaled, w_gate, w_up, w_down):
    gate = contract(xr, w_gate, (2,), (0,))
    up = contract(xr, w_up, (2,), (0,))
    sig = jax.nn.sigmoid(gate)
    act = (gate * sig * up).astype(jnp.bfloat16)
    dh = contract(scaled, w_down, (2,), (1,))
    dgate = (dh * up * sig * (1.0 + gate * (1.0 - sig))).astype(jnp.bfloat16)
    dup = (dh * gate * sig).astype(jnp.bfloat16)
    contrib = (contract(dgate, w_gate, (2,), (1,)) + contract(dup, w_up, (2,), (1,))).astype(
        jnp.bfloat16
    )
    grad_g = contract(xr, dgate, (0, 1), (0, 1)).astype(jnp.bfloat16)
    grad_u = contract(xr, dup, (0, 1), (0, 1)).astype(jnp.bfloat16)
    grad_d = contract(act, scaled, (0, 1), (0, 1)).astype(jnp.bfloat16)
    return contrib, grad_g, grad_u, grad_d


def per_device(tokens, out_grad, expert_ids, route_probs, gate_weight, up_weight, down_weight):
    tok_dev, width = tokens.shape
    top_k = expert_ids.shape[1]
    exp_dev, _, hid = gate_weight.shape
    n_owner = lax.axis_size("expert")
    n_dp = lax.axis_size("dp")
    experts = exp_dev * n_owner
    slots = tok_dev * top_k * 9 // (experts * 8)
    n_slot = experts * slots

    columns = jnp.arange(experts, dtype=jnp.int32)
    onehot = expert_ids[:, :, None] == columns[None, None, :]
    member = jnp.any(onehot, axis=1)
    t_ids = jnp.arange(tok_dev, dtype=jnp.int32)
    lower = (t_ids[None, :] < t_ids[:, None]).astype(jnp.bfloat16)
    before = contract(member.astype(jnp.bfloat16), lower, (0,), (1,)).astype(jnp.int32)
    p_tok = jnp.sum(jnp.where(onehot, route_probs[:, :, None], 0.0), axis=1).T

    r_ids = jnp.arange(slots, dtype=jnp.int32)
    hit = member.T[:, None, :] & (before[:, None, :] == r_ids[None, :, None])
    p_slot = jnp.sum(jnp.where(hit, p_tok[:, None, :], 0.0), axis=2)
    sel = hit.astype(jnp.bfloat16).reshape(n_owner, exp_dev, slots, tok_dev)
    p_slot = p_slot.reshape(n_owner, exp_dev, slots)
    both_in = jnp.concatenate([tokens, out_grad], axis=0)
    zeros = jnp.zeros_like(sel[:, 0])
    ones = jnp.ones((n_owner, slots), jnp.float32)

    contribs = []
    grads = []
    after = None
    for local in range(exp_dev):
        sel_l = sel[:, local]
        pick = jnp.concatenate(
            [jnp.concatenate([sel_l, zeros], axis=2), jnp.concatenate([zeros, sel_l], axis=2)], axis=1
        )
        scale = jnp.concatenate([ones, p_slot[:, local]], axis=1)
        send = (scale[:, :, None] * contract(pick, both_in, (2,), (0,))).astype(jnp.bfloat16)
        recv = lax.all_to_all(send, "expert", split_axis=0, concat_axis=0, tiled=True)
        if after is not None:
            recv, _ = lax.optimization_barrier((recv, after))
        xr = recv[:, :slots]
        scaled = recv[:, slots:]
        contrib, grad_g, grad_u, grad_d = expert_work(
            xr, scaled, gate_weight[local], up_weight[local], down_weight[local]
        )
        reduced = dp_reduce_scatter(pack_grads(grad_g, grad_u, grad_d, n_dp), n_dp)
        after = (contrib, reduced)
        contribs.append(contrib)
        grads.append(reduced.reshape(3, -1))

    back = lax.all_to_all(
        jnp.concatenate(contribs, axis=1), "expert", split_axis=0, concat_axis=0, tiled=True
    )
    sel_all = sel.reshape(n_owner, exp_dev * slots, tok_dev)
    in_grad = contract(sel_all, back, (0, 1), (0, 1)).astype(jnp.bfloat16)

    dsl = width // n_dp
    stack_g = jnp.stack([r[0].reshape(dsl, hid) for r in grads], axis=0)
    stack_u = jnp.stack([r[1].reshape(dsl, hid) for r in grads], axis=0)
    stack_d = jnp.stack([r[2].reshape(hid, dsl) for r in grads], axis=0)
    return (in_grad, stack_g, stack_u, stack_d)


def solution(mesh):
    in_specs = (
        P(("dp", "expert"), None),
        P(("dp", "expert"), None),
        P(("dp", "expert"), None),
        P(("dp", "expert"), None),
        P("expert", None, None),
        P("expert", None, None),
        P("expert", None, None),
    )
    out_specs = (
        P(("dp", "expert"), None),
        P("expert", "dp", None),
        P("expert", "dp", None),
        P("expert", None, "dp"),
    )
    return jax.shard_map(
        per_device, mesh=mesh, in_specs=in_specs, out_specs=out_specs, check_vma=False
    )
```
